128 devices in a mesh: seq: 64 (over y, x, z), head: 2 (over core).
Axes of the slice: x: 4, y: 4, z: 4, core: 2. Of those that a mesh axis runs over, the one named last changes fastest.
Arguments:
- x_in: bfloat16 [32768, 4096], P('seq', 'head'), may hold values from -6 to 6
- gate_input: bfloat16 [32768, 4096], P('seq', 'head'), may hold values from -6 to 6
- in_b: bfloat16 [32768, 512], P('seq', 'head'), may hold values from -2 to 2
- in_c: bfloat16 [32768, 512], P('seq', 'head'), may hold values from -2 to 2
- step_size: float32 [32768, 64], P('seq', 'head'), may hold values from 0.02 to 0.2
- log_decay: float32 [32768, 64], P('seq', 'head'), may hold values from -0.7 to 0, as said below
- skip_gain: float32 [64], P('head'), may hold values from 0.5 to 1.5
- norm_gain: float32 [4096], P('head'), may hold values from 0.5 to 1.5
- out_weight: bfloat16 [4096, 8192], P('head', 'seq'), may hold values from -0.046875 to 0.046875
- probe: bfloat16 [64, 8192, 128], P('seq', 'head'), may hold values from -0.29882812 to 0.29882812
- span_start: int32 [4096], P('seq'), may hold values from 0 to 32767, as said below
- span_len: int32 [4096], P('seq'), may hold values from 1 to 128, as said below
- span_owner: int32 [4096, 1], P('seq'), may hold values from 0 to 63; in each aligned block of 64 rows (0 to 63, 64 to 127, ...) at most 2 rows name the same one
- span_label: int32 [4096], P('seq'), may hold values from 0 to 127
Outputs:
- layer_out: bfloat16 [32768, 8192], P('seq', 'head')
- probe_grad: float32 [64, 8192, 128], P('seq', 'head')
- slot_loss: float32 [64, 128], P('seq')
The draws below stay inside these ranges and needn't reach their ends.
Inputs may be any that keep to these rules, and one draw needn't show every extreme that they name: `log_decay`: log of a decay factor in (0, 1]. Span i starts among tokens (i // 64) * 512 to (i // 64 + 1) * 512 - 1, and span_start + span_len <= 32768. `span_len`: the first span of every block of 64 spans is 128 long. `span_owner`: in each aligned block of 64 spans no owner appears more than 2 times.
All inputs are finite; a program needn't handle non-finite values.
Results may differ from the reference program's by a relative error of at most 0.0068.
Values may be sent and summed in bfloat16 or wider, within the bound.
No kernel may reach another device: no remote copies, remote signals or barrier semaphores. Data moves between devices by JAX's collectives and lax.ppermute only.
A program may use at most 256 MiB of HBM per device.

```python
import math
import jax
import jax.numpy as jnp
import numpy as np
from jax import lax

D = 8192
HEADS = 64
HEAD_DIM = 64
STATE = 128
GROUPS = 4
LABELS = 128
TOK_DEV = 512
SPAN_DEV = 64
CAP = 2
SPAN_MAX = 128
INNER = 4096
TOKENS = 32768
SPANS = 4096
SLOTS = 128
N_SEQ = 64
N_HEAD = 2


def draw_log_decay(key, part):
    keys = jax.random.split(key, 6)
    slow = jax.random.randint(keys[0], (HEADS,), 0, 10) < 5
    rate_slow = jnp.exp(jax.random.uniform(keys[1], (HEADS,), jnp.float32, math.log(0.1 / TOKENS), math.log(0.5 / TOKENS)))
    rate_fast = jnp.exp(jax.random.uniform(keys[2], (HEADS,), jnp.float32, math.log(1.0 / 50.0), math.log(1.0 / 15.0)))
    forgetting_speed = jnp.where(slow, rate_slow, rate_fast)
    approximate_guess = jax.random.uniform(keys[3], (TOKENS, HEADS), jnp.float32, 0.5, 1.5)
    places = jax.random.randint(keys[4], (3,), 0, TOKENS)
    stacking_level = jax.random.uniform(keys[5], (3, HEADS), jnp.float32, 0.22, 0.5)
    interval_covered_flags = (jnp.arange(TOKENS)[:, None] == places[None, :]).astype(jnp.float32)
    spike_magnitude = jnp.dot(interval_covered_flags, stacking_level)
    return -(forgetting_speed[None, :] * approximate_guess + spike_magnitude)


def span_pair(key):
    inner = jax.random.fold_in(key, 7)
    keys = jax.random.split(inner, 2)
    offsets = jax.random.randint(keys[0], (N_SEQ, SPAN_DEV), 0, TOK_DEV)
    lengths = jax.random.randint(keys[1], (N_SEQ, SPAN_DEV), 1, SPAN_MAX + 1)
    lengths = lengths.at[:, 0].set(SPAN_MAX)
    starts = jnp.arange(N_SEQ, dtype=jnp.int32)[:, None] * TOK_DEV + offsets
    starts = jnp.minimum(starts, TOKENS - lengths)
    return (starts.reshape(-1).astype(jnp.int32), lengths.reshape(-1).astype(jnp.int32))


def draw_span_start(key, part):
    return span_pair(key)[0]


def draw_span_len(key, part):
    return span_pair(key)[1]


def plant(array, rng, smallest, largest):
    index_at = [jax.random.randint(jax.random.fold_in(rng, axis), (), 0, length) for axis, length in enumerate(array.shape)]
    main_axis = array.shape.index(max(array.shape))
    neighbour = index_at[:main_axis] + [(index_at[main_axis] + 1) % array.shape[main_axis]] + index_at[main_axis + 1:]
    return array.at[tuple(index_at)].set(smallest).at[tuple(neighbour)].set(largest)


def block_scale(rng, extent, pieces, low, high):
    def one(position, parts):
        draws = jax.random.uniform(jax.random.fold_in(jax.random.fold_in(rng, 6), position), (parts,), jnp.float32, low / len(pieces), high / len(pieces))
        return jnp.repeat(jnp.exp(draws), extent[position] // parts).reshape((-1,) + (1,) * (len(extent) - position - 1))

    loudness = one(*pieces[0])
    for cut in pieces[1:]:
        loudness = loudness * one(*cut)
    return loudness


def shared_out(rng, own, number, rows, count, top, limit, slope):
    ranking = jax.random.permutation(rng, count)
    heavy_load, usual = shares(count, rows * top, limit, slope, True), shares(count, rows * top, limit, slope, False)
    places = jnp.arange(count)

    def named(tallies, turn):
        used = int((tallies > 0).sum())
        fixed = max(1, used // 4)
        moved = fixed + (places - fixed + turn * (used - fixed)) % max(1, count - fixed)
        return jnp.zeros((count,), jnp.int32).at[ranking[jnp.where(places < fixed, places, moved)]].set(jnp.asarray(tallies, jnp.int32))

    tallies = jnp.where(number % 4 == 0, named(heavy_load, number // 4), named(usual, number - number // 4 - 1))
    mixed = jax.random.permutation(jax.random.fold_in(own, 3), count)
    source_of, taker = mixed[0:count // 2 * 2:2], mixed[1:count // 2 * 2:2]
    slack = jnp.minimum(tallies[source_of] - 1, limit - tallies[taker]) // 2
    slack = jnp.where((source_of == ranking[0]) | (taker == ranking[0]) | (tallies[taker] == 0), 0, jnp.maximum(slack, 0))
    moved = jax.random.randint(jax.random.fold_in(own, 4), (count // 2,), 0, 1 << 20) % (slack + 1)
    tallies = tallies.at[source_of].add(-moved).at[taker].add(moved)
    items = jnp.searchsorted(jnp.cumsum(tallies), jnp.arange(rows * top), side="right").astype(jnp.int32)
    listing = items.reshape(top, rows).T
    listing = listing[jax.random.permutation(jax.random.fold_in(own, 1), rows)]
    turn = jax.random.randint(jax.random.fold_in(own, 2), (rows, 1), 0, top)
    return jnp.take_along_axis(listing, (jnp.arange(top)[None, :] + turn) % top, axis=1)


def shares(amount, total, reach, lean, full):
    weights = [(1 << 20) // math.isqrt(grade ** lean) + 1 for grade in range(1, amount + 1)]
    largest = reach if full else min(reach, max(-(-total // amount), total * weights[0] // sum(weights)))
    least = 1 if total - largest >= amount - 1 else 0
    given, rest = [largest] + [least] * (amount - 1), total - largest - least * (amount - 1)
    while rest > 0:
        candidates = [i for i in range(1, amount) if given[i] < largest] or [i for i in range(1, amount) if given[i] < reach]
        whole, remaining = sum([weights[i] for i in candidates]), rest
        for i in candidates:
            more = min(reach - given[i], max(1, remaining * weights[i] // whole), rest)
            given[i] = given[i] + more
            rest = rest - more
    return np.array(given)


def noise(stream_key, dims, width, bound, cuts=(), kind=jnp.bfloat16):
    gain = block_scale(stream_key, dims, cuts, -0.22, 0.18) if cuts else 1.0
    values = jax.random.normal(stream_key, dims, jnp.float32) * width * gain
    return jnp.minimum(jnp.maximum(values, -bound), bound).astype(kind)


def setup_inputs(seed: int = 0) -> dict:
    streams_of = jax.random.split(jax.random.key(seed), 15)
    x_in = noise(streams_of[0], (TOKENS, INNER), 1.0, 6.0, ((0, 64), (1, 2)))
    gate_input = noise(streams_of[1], (TOKENS, INNER), 1.0, 6.0, ((0, 64), (1, 2)))
    in_b = noise(streams_of[2], (TOKENS, GROUPS * STATE), 0.3, 2.0, ((0, 64), (1, 2)))
    in_c = noise(streams_of[3], (TOKENS, GROUPS * STATE), 0.3, 2.0, ((0, 64), (1, 2)))
    step_size = jnp.clip(jnp.exp(math.log(0.2) - 2.3025851 * jax.random.uniform(streams_of[4], (TOKENS, HEADS), jnp.float32) ** block_scale(streams_of[4], (TOKENS, HEADS), ((0, 64), (1, 2)), -0.2, 0.2)), 0.02, 0.2)
    log_decay = draw_log_decay(jax.random.fold_in(streams_of[14], 71), 0)
    skip_gain = jnp.clip(0.5 + 1.0 * jax.random.uniform(streams_of[6], (HEADS,), jnp.float32) ** block_scale(streams_of[6], (HEADS,), ((0, 2),), -0.2, 0.2), 0.5, 1.5)
    norm_gain = jnp.clip(1.0 + 0.1 * jax.random.normal(streams_of[7], (INNER,), jnp.float32), 0.5, 1.5)
    out_weight = noise(streams_of[8], (INNER, D), (4 * INNER) ** -0.5, 0.046875, ((0, 2), (1, 64)))
    probe = noise(streams_of[9], (N_SEQ, D, LABELS), 0.05, 0.29882812, ((0, 64), (1, 2)))
    span_start = draw_span_start(jax.random.fold_in(streams_of[14], 71), 0)
    span_len = draw_span_len(jax.random.fold_in(streams_of[14], 71), 0)
    span_owner_keys = jax.random.split(jax.random.fold_in(streams_of[12], 1), SPANS // SPAN_DEV)
    span_owner_turns = jax.random.permutation(jax.random.fold_in(streams_of[12], 3), SPANS // SPAN_DEV)
    span_owner = jax.vmap(lambda own, number: shared_out(jax.random.fold_in(streams_of[12], 2), own, number, SPAN_DEV, N_SEQ, 1, CAP, 2))(span_owner_keys, span_owner_turns).reshape((SPANS, 1))
    span_label = plant(jax.random.randint(streams_of[13], (SPANS,), 0, LABELS), jax.random.fold_in(streams_of[13], 1), 0, LABELS - 1).astype(jnp.int32)
    return {"x_in": x_in, "gate_input": gate_input, "in_b": in_b, "in_c": in_c, "step_size": step_size, "log_decay": log_decay, "skip_gain": skip_gain, "norm_gain": norm_gain, "out_weight": out_weight, "probe": probe, "span_start": span_start, "span_len": span_len, "span_owner": span_owner, "span_label": span_label}


def segment_summands(xs, bmat, cmat, dtk, cum):
    high = lax.Precision.HIGHEST
    tok = xs.shape[0]
    cb = jnp.einsum('tgn,sgn->gts', cmat, bmat, precision=high)
    ordered = jnp.transpose(cum, (1, 2, 0))
    diff = ordered[:, :, :, None] - ordered[:, :, None, :]
    lower = jnp.arange(tok)[:, None] >= jnp.arange(tok)[None, :]
    decay = jnp.where(lower, jnp.exp(jnp.where(lower, diff, 0.0)), 0.0)
    weights = cb[:, None] * decay * jnp.transpose(dtk, (1, 2, 0))[:, :, None, :]
    intra = jnp.einsum('gkts,sgkp->tgkp', weights, xs, precision=high)
    tail = jnp.exp(cum[-1][None] - cum) * dtk
    local_state = jnp.einsum('tgk,tgkp,tgn->gkpn', tail, xs, bmat, precision=high)
    return (intra, local_state, cum[-1])

def inter_term(cmat, cum, state_in):
    high = lax.Precision.HIGHEST
    return jnp.exp(cum)[..., None] * jnp.einsum('tgn,gkpn->tgkp', cmat, state_in, precision=high)

def reference(x_in, gate_input, in_b, in_c, step_size, log_decay, skip_gain, norm_gain, out_weight, probe, span_start, span_len, span_owner, span_label):
    per_group = HEADS // GROUPS
    xs = x_in.astype(jnp.float32).reshape(N_SEQ, TOK_DEV, GROUPS, per_group, HEAD_DIM)
    bmat = in_b.astype(jnp.float32).reshape(N_SEQ, TOK_DEV, GROUPS, STATE)
    cmat = in_c.astype(jnp.float32).reshape(N_SEQ, TOK_DEV, GROUPS, STATE)
    dtk = step_size.reshape(N_SEQ, TOK_DEV, GROUPS, per_group)
    cum = jnp.cumsum(log_decay.reshape(N_SEQ, TOK_DEV, GROUPS, per_group), axis=1)

    def advance(state, block):
        xb, bb, cb, db, qb = block
        intra, local_state, total = segment_summands(xb, bb, cb, db, qb)
        result = intra + inter_term(cb, qb, state)
        fresh = state * jnp.exp(total)[..., None, None] + local_state
        return (fresh, result)
    start_state = jnp.zeros((GROUPS, per_group, HEAD_DIM, STATE), jnp.float32)
    unused, ssm = lax.scan(advance, start_state, (xs, bmat, cmat, dtk, cum))
    ssm = ssm + skip_gain.reshape(GROUPS, per_group)[None, None, :, :, None] * xs
    ssm = ssm.reshape(TOKENS, GROUPS, per_group * HEAD_DIM)
    gated = ssm * jax.nn.silu(gate_input.astype(jnp.float32).reshape(TOKENS, GROUPS, per_group * HEAD_DIM))
    meansq = lax.optimization_barrier(jnp.mean(gated * gated, axis=-1, keepdims=True))
    normalized_input = gated * lax.rsqrt(meansq + 1e-05)
    y_out = (normalized_input.reshape(TOKENS, INNER) * norm_gain[None, :]).astype(jnp.bfloat16)
    rows_half = INNER // N_HEAD
    total = jnp.zeros((TOKENS, D), jnp.float32)
    for half in range(N_HEAD):
        part = jnp.dot(y_out[:, half * rows_half:(half + 1) * rows_half], out_weight[half * rows_half:(half + 1) * rows_half], preferred_element_type=jnp.float32)
        part = lax.optimization_barrier(part.astype(jnp.bfloat16)).astype(jnp.float32)
        total = total + part
    layer_out = total.astype(jnp.bfloat16)
    padded = jnp.concatenate([layer_out, jnp.zeros((SPAN_MAX, D), jnp.bfloat16)], axis=0)

    def pool(pair):
        first, length = pair
        rows = lax.dynamic_slice_in_dim(padded, first.astype(jnp.int32), SPAN_MAX, 0).astype(jnp.float32)
        keep = jnp.arange(SPAN_MAX) < length
        return lax.optimization_barrier(jnp.sum(jnp.where(keep[:, None], rows, 0.0), axis=0))
    sums = lax.map(pool, (span_start, span_len))
    feature = (sums / span_len[:, None].astype(jnp.float32)).astype(jnp.bfloat16)
    owners = span_owner[:, 0].reshape(N_SEQ, SPAN_DEV)
    index = jnp.arange(SPAN_DEV)
    earlier = index[None, :] < index[:, None]
    same = owners[:, :, None] == owners[:, None, :]
    slot = lax.optimization_barrier(jnp.sum(jnp.logical_and(same, earlier[None]), axis=-1)).astype(jnp.int32)
    matrix_column_index = (jnp.arange(N_SEQ, dtype=jnp.int32)[:, None] * CAP + slot).reshape(-1).astype(jnp.int32)
    table = jnp.full((N_SEQ, SLOTS), -1, jnp.int32).at[span_owner[:, 0], matrix_column_index].set(jnp.arange(SPANS, dtype=jnp.int32))

    def score(owner):
        ids = table[owner]
        valid = ids >= 0
        safe = jnp.maximum(ids, 0)
        feats = jnp.where(valid[:, None], feature[safe], jnp.zeros((), jnp.bfloat16))
        labels = jnp.where(valid, span_label[safe], -1)
        logits = jnp.dot(feats, probe[owner], preferred_element_type=jnp.float32)
        top = lax.optimization_barrier(jnp.max(logits, axis=1, keepdims=True))
        lse = top[:, 0] + jnp.log(lax.optimization_barrier(jnp.sum(jnp.exp(logits - top), axis=1)))
        onehot = jnp.arange(LABELS)[None, :] == labels[:, None]
        picked = lax.optimization_barrier(jnp.sum(jnp.where(onehot, logits, 0.0), axis=1))
        loss = jnp.where(valid, lse - picked, 0.0)
        probs = jnp.exp(logits - lse[:, None])
        resid = jnp.where(valid[:, None], probs - onehot.astype(jnp.float32), 0.0).astype(jnp.bfloat16)
        grad = jnp.dot(feats.T, resid, preferred_element_type=jnp.float32)
        return (grad, loss)
    probe_grad, slot_loss = lax.map(score, jnp.arange(N_SEQ, dtype=jnp.int32))
    return (layer_out, probe_grad, slot_loss)
```

```python
import jax
import jax.numpy as jnp
from jax import lax
from jax.sharding import PartitionSpec as P

HEAD_DIM = 64
STATE = 128
CAP = 2


def from_behind(value, axis, steps):
    count = lax.axis_size(axis)
    leading, last = (max(0, -steps), min(count, count - steps))
    return lax.ppermute(value, axis, [(source, source + steps) for source in range(leading, last)])


def segment_summands(xs, bmat, cmat, dtk, cum):
    high = lax.Precision.HIGHEST
    tok = xs.shape[0]
    cb = jnp.einsum("tgn,sgn->gts", cmat, bmat, precision=high)
    ordered = jnp.transpose(cum, (1, 2, 0))
    diff = ordered[:, :, :, None] - ordered[:, :, None, :]
    lower = jnp.arange(tok)[:, None] >= jnp.arange(tok)[None, :]
    decay = jnp.where(lower, jnp.exp(jnp.where(lower, diff, 0.0)), 0.0)
    weights = cb[:, None] * decay * jnp.transpose(dtk, (1, 2, 0))[:, :, None, :]
    intra = jnp.einsum("gkts,sgkp->tgkp", weights, xs, precision=high)
    tail = jnp.exp(cum[-1][None] - cum) * dtk
    local_state = jnp.einsum("tgk,tgkp,tgn->gkpn", tail, xs, bmat, precision=high)
    return (intra, local_state, cum[-1])


def inter_term(cmat, cum, state_in):
    high = lax.Precision.HIGHEST
    return jnp.exp(cum)[..., None] * jnp.einsum("tgn,gkpn->tgkp", cmat, state_in, precision=high)


def piecewise_terms(xs, bmat, cmat, dtk, logd):
    tok = xs.shape[0]
    width = min(tok, 256)
    pieces = tok // width
    state = jnp.zeros((xs.shape[1], xs.shape[2], xs.shape[3], bmat.shape[2]), jnp.float32)
    total = jnp.zeros((xs.shape[1], xs.shape[2]), jnp.float32)
    results = []
    for piece in range(pieces):
        lower_edge = piece * width
        upper_edge = lower_edge + width
        inner_cum = jnp.cumsum(logd[lower_edge:upper_edge], axis=0)
        intra, local_state, piece_total = segment_summands(
            xs[lower_edge:upper_edge],
            bmat[lower_edge:upper_edge],
            cmat[lower_edge:upper_edge],
            dtk[lower_edge:upper_edge],
            inner_cum,
        )
        results.append(intra + inter_term(cmat[lower_edge:upper_edge], inner_cum, state))
        state = state * jnp.exp(piece_total)[..., None, None] + local_state
        total = total + piece_total
    return (jnp.concatenate(results, axis=0), state, total)


def exclusive_scan(part, axis):
    count = lax.axis_size(axis)
    place = lax.axis_index(axis)
    inclusive = part
    exclusive = None
    step = 1
    while step < count:
        pairs = [(source, source + step) for source in range(count - step)]
        got = jax.tree.map(lambda a: lax.ppermute(a, axis, pairs), inclusive)
        exclusive = got if exclusive is None else combine_states(got, exclusive)
        if step * 2 < count:
            inclusive = combine_states(got, inclusive)
        step *= 2
    return exclusive[0]

def combine_states(earlier, later):
    return (earlier[0] * jnp.exp(later[1])[..., None, None] + later[0], earlier[1] + later[1])


def inside_mask(first, length, place):
    return jnp.logical_and(
        place[None, :] >= first[:, None], place[None, :] < (first + length)[:, None]
    ).astype(jnp.bfloat16)


def on_device(
    x_in,
    gate_input,
    in_b,
    in_c,
    step_size,
    log_decay,
    skip_gain,
    norm_gain,
    out_weight,
    probe,
    span_start,
    span_len,
    span_owner,
    span_label,
):
    tok = x_in.shape[0]
    local_attention_heads = step_size.shape[1]
    groups_here = in_b.shape[1] // STATE
    per_group = local_attention_heads // groups_here
    xs = x_in.astype(jnp.float32).reshape(tok, groups_here, per_group, HEAD_DIM)
    bmat = in_b.astype(jnp.float32).reshape(tok, groups_here, STATE)
    cmat = in_c.astype(jnp.float32).reshape(tok, groups_here, STATE)
    dtk = step_size.reshape(tok, groups_here, per_group)
    logd = log_decay.reshape(tok, groups_here, per_group)
    cum = jnp.cumsum(logd, axis=0)
    intra, local_state, total = piecewise_terms(xs, bmat, cmat, dtk, logd)
    state_in = exclusive_scan((local_state, total), "seq")
    ssm = (
        intra
        + inter_term(cmat, cum, state_in)
        + skip_gain.reshape(groups_here, per_group)[None, :, :, None] * xs
    )
    ssm = ssm.reshape(tok, groups_here, per_group * HEAD_DIM)
    gated = ssm * jax.nn.silu(
        gate_input.astype(jnp.float32).reshape(tok, groups_here, per_group * HEAD_DIM)
    )
    meansq = jnp.mean(gated * gated, axis=-1, keepdims=True)
    normalized_input = gated * lax.rsqrt(meansq + 1e-05)
    y_out = (normalized_input.reshape(tok, -1) * norm_gain[None, :]).astype(jnp.bfloat16)
    partial_out = jnp.dot(
        y_out,
        lax.all_gather(out_weight, "seq", axis=1, tiled=True),
        preferred_element_type=jnp.float32,
    )
    layer_out = lax.psum_scatter(
        partial_out.astype(jnp.bfloat16), "head", scatter_dimension=1, tiled=True
    )
    base = lax.axis_index("seq") * tok
    reach = min(tok, 128)
    following = from_behind(layer_out[:reach], "seq", -1)
    rows = jnp.concatenate([layer_out, following], axis=0)
    place = base + jnp.arange(tok + reach, dtype=jnp.int32)
    sums = jnp.dot(
        inside_mask(span_start, span_len, place), rows, preferred_element_type=jnp.float32
    )
    own_feature = (sums / span_len[:, None].astype(jnp.float32)).astype(jnp.bfloat16)
    count = span_start.shape[0]
    owners = lax.axis_size("seq")
    slots_total = owners * CAP
    owner = span_owner[:, 0]
    index = jnp.arange(count)
    earlier = index[None, :] < index[:, None]
    same = owner[:, None] == owner[None, :]
    slot = jnp.sum(jnp.logical_and(same, earlier), axis=1)
    target_labels = owner * CAP + slot
    pick = jnp.arange(slots_total, dtype=jnp.int32)[:, None] == target_labels[None, :]
    label_col = jnp.zeros((count, 128), jnp.bfloat16).at[:, 0].set(
        span_label.astype(jnp.bfloat16)
    )
    packed = jnp.concatenate([own_feature, label_col], axis=1)
    width = own_feature.shape[1]
    empty = jnp.zeros((1, packed.shape[1]), jnp.bfloat16).at[0, width].set(-1.0)
    chosen = jnp.where(jnp.any(pick, axis=1), jnp.argmax(pick, axis=1), count)
    send = jnp.concatenate([packed, empty], axis=0)[chosen].reshape(owners, CAP, -1)
    got = lax.all_to_all(send, "seq", split_axis=0, concat_axis=0, tiled=True)
    got = got.reshape(slots_total, -1)
    feature = got[:, :width]
    labels = got[:, width].astype(jnp.int32)
    valid = labels >= 0
    partial_logits = jnp.dot(feature, probe[0], preferred_element_type=jnp.float32)
    logits = partial_logits + lax.ppermute(partial_logits, "head", [(0, 1), (1, 0)])
    top = jnp.max(logits, axis=1, keepdims=True)
    lse = top[:, 0] + jnp.log(jnp.sum(jnp.exp(logits - top), axis=1))
    onehot = jnp.arange(logits.shape[1])[None, :] == labels[:, None]
    picked = jnp.sum(jnp.where(onehot, logits, 0.0), axis=1)
    loss = jnp.where(valid, lse - picked, 0.0)
    probs = jnp.exp(logits - lse[:, None])
    resid = jnp.where(valid[:, None], probs - onehot.astype(jnp.float32), 0.0).astype(jnp.bfloat16)
    grad = jnp.dot(feature.T, resid, preferred_element_type=jnp.float32)
    return (layer_out, grad[None], loss[None])


def solution(mesh):
    placed = (
        P("seq", "head"),
        P("seq", "head"),
        P("seq", "head"),
        P("seq", "head"),
        P("seq", "head"),
        P("seq", "head"),
        P("head"),
        P("head"),
        P("head", "seq"),
        P("seq", "head", None),
        P("seq"),
        P("seq"),
        P("seq", None),
        P("seq"),
    )
    return jax.shard_map(
        on_device,
        mesh=mesh,
        in_specs=placed,
        out_specs=(P("seq", "head"), P("seq", "head", None), P("seq", None)),
        check_vma=False,
    )
```

```python
import jax
import jax.numpy as jnp
from jax import lax
from jax.sharding import PartitionSpec as P

HEAD_DIM = 64
STATE = 128
CAP = 2


def from_behind(value, axis, steps):
    count = lax.axis_size(axis)
    leading, last = (max(0, -steps), min(count, count - steps))
    return lax.ppermute(value, axis, [(source, source + steps) for source in range(leading, last)])


def segment_summands(xs, bmat, cmat, dtk, cum):
    high = lax.Precision.HIGHEST
    tok = xs.shape[0]
    cb = jnp.einsum("tgn,sgn->gts", cmat, bmat, precision=high)
    ordered = jnp.transpose(cum, (1, 2, 0))
    diff = ordered[:, :, :, None] - ordered[:, :, None, :]
    lower = jnp.arange(tok)[:, None] >= jnp.arange(tok)[None, :]
    decay = jnp.where(lower, jnp.exp(jnp.where(lower, diff, 0.0)), 0.0)
    weights = cb[:, None] * decay * jnp.transpose(dtk, (1, 2, 0))[:, :, None, :]
    intra = jnp.einsum("gkts,sgkp->tgkp", weights, xs, precision=high)
    tail = jnp.exp(cum[-1][None] - cum) * dtk
    local_state = jnp.einsum("tgk,tgkp,tgn->gkpn", tail, xs, bmat, precision=high)
    return (intra, local_state, cum[-1])


def inter_term(cmat, cum, state_in):
    high = lax.Precision.HIGHEST
    return jnp.exp(cum)[..., None] * jnp.einsum("tgn,gkpn->tgkp", cmat, state_in, precision=high)


def piecewise_terms(xs, bmat, cmat, dtk, logd):
    tok = xs.shape[0]
    width = min(tok, 256)
    pieces = tok // width
    state = jnp.zeros((xs.shape[1], xs.shape[2], xs.shape[3], bmat.shape[2]), jnp.float32)
    total = jnp.zeros((xs.shape[1], xs.shape[2]), jnp.float32)
    results = []
    for piece in range(pieces):
        lower_edge = piece * width
        upper_edge = lower_edge + width
        inner_cum = jnp.cumsum(logd[lower_edge:upper_edge], axis=0)
        intra, local_state, piece_total = segment_summands(
            xs[lower_edge:upper_edge],
            bmat[lower_edge:upper_edge],
            cmat[lower_edge:upper_edge],
            dtk[lower_edge:upper_edge],
            inner_cum,
        )
        results.append(intra + inter_term(cmat[lower_edge:upper_edge], inner_cum, state))
        state = state * jnp.exp(piece_total)[..., None, None] + local_state
        total = total + piece_total
    return (jnp.concatenate(results, axis=0), state, total)


def exclusive_scan(part, axis):
    count = lax.axis_size(axis)
    place = lax.axis_index(axis)
    inclusive = part
    exclusive = None
    step = 1
    while step < count:
        pairs = [(source, source + step) for source in range(count - step)]
        got = jax.tree.map(lambda a: lax.ppermute(a, axis, pairs), inclusive)
        exclusive = got if exclusive is None else combine_states(got, exclusive)
        if step * 2 < count:
            inclusive = combine_states(got, inclusive)
        step *= 2
    return exclusive[0]

def combine_states(earlier, later):
    return (earlier[0] * jnp.exp(later[1])[..., None, None] + later[0], earlier[1] + later[1])


def head_sum(part, axis):
    half = part.shape[1] // 2
    me = lax.axis_index(axis)
    mine = lax.dynamic_slice_in_dim(part, me * half, half, axis=1)
    other = lax.dynamic_slice_in_dim(part, (1 - me) * half, half, axis=1)
    got = lax.ppermute(other, axis, [(0, 1), (1, 0)])
    return (mine.astype(jnp.float32) + got.astype(jnp.float32)).astype(jnp.bfloat16)

def inside_mask(first, length, place):
    return jnp.logical_and(
        place[None, :] >= first[:, None], place[None, :] < (first + length)[:, None]
    ).astype(jnp.bfloat16)


def on_device(
    x_in,
    gate_input,
    in_b,
    in_c,
    step_size,
    log_decay,
    skip_gain,
    norm_gain,
    out_weight,
    probe,
    span_start,
    span_len,
    span_owner,
    span_label,
):
    tok = x_in.shape[0]
    local_attention_heads = step_size.shape[1]
    groups_here = in_b.shape[1] // STATE
    per_group = local_attention_heads // groups_here
    xs = x_in.astype(jnp.float32).reshape(tok, groups_here, per_group, HEAD_DIM)
    bmat = in_b.astype(jnp.float32).reshape(tok, groups_here, STATE)
    cmat = in_c.astype(jnp.float32).reshape(tok, groups_here, STATE)
    dtk = step_size.reshape(tok, groups_here, per_group)
    logd = log_decay.reshape(tok, groups_here, per_group)
    cum = jnp.cumsum(logd, axis=0)
    intra, local_state, total = piecewise_terms(xs, bmat, cmat, dtk, logd)
    state_in = exclusive_scan((local_state, total), "seq")
    ssm = (
        intra
        + inter_term(cmat, cum, state_in)
        + skip_gain.reshape(groups_here, per_group)[None, :, :, None] * xs
    )
    ssm = ssm.reshape(tok, groups_here, per_group * HEAD_DIM)
    gated = ssm * jax.nn.silu(
        gate_input.astype(jnp.float32).reshape(tok, groups_here, per_group * HEAD_DIM)
    )
    meansq = jnp.mean(gated * gated, axis=-1, keepdims=True)
    normalized_input = gated * lax.rsqrt(meansq + 1e-05)
    y_out = (normalized_input.reshape(tok, -1) * norm_gain[None, :]).astype(jnp.bfloat16)
    rows_here = out_weight.shape[0]
    cut = rows_here // 2
    upper_weight = lax.all_gather(out_weight[:cut], "seq", axis=1, tiled=True)
    lower_weight = lax.all_gather(out_weight[cut:], "seq", axis=1, tiled=True)
    early = jnp.dot(y_out[:, :cut], upper_weight, preferred_element_type=jnp.float32)
    reach = min(tok, 128)

    def project(first, last):
        part = early[first:last] + jnp.dot(
            y_out[first:last, cut:], lower_weight, preferred_element_type=jnp.float32
        )
        return head_sum(part.astype(jnp.bfloat16), "head")

    head_rows = project(0, reach)
    following = from_behind(head_rows, "seq", -1)
    layer_out = jnp.concatenate([head_rows, project(reach, tok)], axis=0)
    base = lax.axis_index("seq") * tok
    place = base + jnp.arange(tok + reach, dtype=jnp.int32)
    mask = inside_mask(span_start, span_len, place)
    sums = jnp.dot(mask[:, :tok], layer_out, preferred_element_type=jnp.float32) + jnp.dot(
        mask[:, tok:], following, preferred_element_type=jnp.float32
    )
    own_feature = (sums / span_len[:, None].astype(jnp.float32)).astype(jnp.bfloat16)
    count = span_start.shape[0]
    owners = lax.axis_size("seq")
    slots_total = owners * CAP
    owner = span_owner[:, 0]
    index = jnp.arange(count)
    earlier = index[None, :] < index[:, None]
    same = owner[:, None] == owner[None, :]
    slot = jnp.sum(jnp.logical_and(same, earlier), axis=1)
    target_labels = owner * CAP + slot
    pick = jnp.arange(slots_total, dtype=jnp.int32)[:, None] == target_labels[None, :]
    label_col = jnp.zeros((count, 128), jnp.bfloat16).at[:, 0].set(
        span_label.astype(jnp.bfloat16)
    )
    packed = jnp.concatenate([own_feature, label_col], axis=1)
    width = own_feature.shape[1]
    empty = jnp.zeros((1, packed.shape[1]), jnp.bfloat16).at[0, width].set(-1.0)
    chosen = jnp.where(jnp.any(pick, axis=1), jnp.argmax(pick, axis=1), count)
    send = jnp.concatenate([packed, empty], axis=0)[chosen].reshape(owners, CAP, -1)
    got = lax.all_to_all(send, "seq", split_axis=0, concat_axis=0, tiled=True)
    got = got.reshape(slots_total, -1)
    feature = got[:, :width]
    labels = got[:, width].astype(jnp.int32)
    valid = labels >= 0
    partial_logits = jnp.dot(feature, probe[0], preferred_element_type=jnp.float32)
    logits = partial_logits + lax.ppermute(partial_logits, "head", [(0, 1), (1, 0)])
    top = jnp.max(logits, axis=1, keepdims=True)
    lse = top[:, 0] + jnp.log(jnp.sum(jnp.exp(logits - top), axis=1))
    onehot = jnp.arange(logits.shape[1])[None, :] == labels[:, None]
    picked = jnp.sum(jnp.where(onehot, logits, 0.0), axis=1)
    loss = jnp.where(valid, lse - picked, 0.0)
    probs = jnp.exp(logits - lse[:, None])
    resid = jnp.where(valid[:, None], probs - onehot.astype(jnp.float32), 0.0).astype(jnp.bfloat16)
    grad = jnp.dot(feature.T, resid, preferred_element_type=jnp.float32)
    return (layer_out, grad[None], loss[None])


def solution(mesh):
    placed = (
        P("seq", "head"),
        P("seq", "head"),
        P("seq", "head"),
        P("seq", "head"),
        P("seq", "head"),
        P("seq", "head"),
        P("head"),
        P("head"),
        P("head", "seq"),
        P("seq", "head", None),
        P("seq"),
        P("seq"),
        P("seq", None),
        P("seq"),
    )
    return jax.shard_map(
        on_device,
        mesh=mesh,
        in_specs=placed,
        out_specs=(P("seq", "head"), P("seq", "head", None), P("seq", None)),
        check_vma=False,
    )
```

```python
import jax
import jax.numpy as jnp
from jax import lax
from jax.sharding import PartitionSpec as P

HEAD_DIM = 64
STATE = 128
CAP = 2


def from_behind(value, axis, steps):
    count = lax.axis_size(axis)
    leading, last = (max(0, -steps), min(count, count - steps))
    return lax.ppermute(value, axis, [(source, source + steps) for source in range(leading, last)])


def segment_summands(xs, bmat, cmat, dtk, cum):
    high = lax.Precision.HIGHEST
    tok = xs.shape[0]
    cb = jnp.einsum("tgn,sgn->gts", cmat, bmat, precision=high)
    ordered = jnp.transpose(cum, (1, 2, 0))
    diff = ordered[:, :, :, None] - ordered[:, :, None, :]
    lower = jnp.arange(tok)[:, None] >= jnp.arange(tok)[None, :]
    decay = jnp.where(lower, jnp.exp(jnp.where(lower, diff, 0.0)), 0.0)
    weights = cb[:, None] * decay * jnp.transpose(dtk, (1, 2, 0))[:, :, None, :]
    intra = jnp.einsum("gkts,sgkp->tgkp", weights, xs, precision=high)
    tail = jnp.exp(cum[-1][None] - cum) * dtk
    local_state = jnp.einsum("tgk,tgkp,tgn->gkpn", tail, xs, bmat, precision=high)
    return (intra, local_state, cum[-1])


def inter_term(cmat, cum, state_in):
    high = lax.Precision.HIGHEST
    return jnp.exp(cum)[..., None] * jnp.einsum("tgn,gkpn->tgkp", cmat, state_in, precision=high)


def piecewise_terms(xs, bmat, cmat, dtk, logd):
    tok = xs.shape[0]
    width = min(tok, 256)
    pieces = tok // width
    state = jnp.zeros((xs.shape[1], xs.shape[2], xs.shape[3], bmat.shape[2]), jnp.float32)
    total = jnp.zeros((xs.shape[1], xs.shape[2]), jnp.float32)
    results = []
    for piece in range(pieces):
        lower_edge = piece * width
        upper_edge = lower_edge + width
        inner_cum = jnp.cumsum(logd[lower_edge:upper_edge], axis=0)
        intra, local_state, piece_total = segment_summands(
            xs[lower_edge:upper_edge],
            bmat[lower_edge:upper_edge],
            cmat[lower_edge:upper_edge],
            dtk[lower_edge:upper_edge],
            inner_cum,
        )
        results.append(intra + inter_term(cmat[lower_edge:upper_edge], inner_cum, state))
        state = state * jnp.exp(piece_total)[..., None, None] + local_state
        total = total + piece_total
    return (jnp.concatenate(results, axis=0), state, total)


def exclusive_scan(part, axis):
    count = lax.axis_size(axis)
    place = lax.axis_index(axis)
    inclusive = part
    exclusive = None
    step = 1
    while step < count:
        pairs = [(source, source + step) for source in range(count - step)]
        got = jax.tree.map(lambda a: lax.ppermute(a, axis, pairs), inclusive)
        exclusive = got if exclusive is None else combine_states(got, exclusive)
        if step * 2 < count:
            inclusive = combine_states(got, inclusive)
        step *= 2
    return exclusive[0]

def combine_states(earlier, later):
    return (earlier[0] * jnp.exp(later[1])[..., None, None] + later[0], earlier[1] + later[1])


def head_sum(part, axis):
    half = part.shape[1] // 2
    me = lax.axis_index(axis)
    mine = lax.dynamic_slice_in_dim(part, me * half, half, axis=1)
    other = lax.dynamic_slice_in_dim(part, (1 - me) * half, half, axis=1)
    got = lax.ppermute(other, axis, [(0, 1), (1, 0)])
    return (mine.astype(jnp.float32) + got.astype(jnp.float32)).astype(jnp.bfloat16)

def inside_mask(first, length, place):
    return jnp.logical_and(
        place[None, :] >= first[:, None], place[None, :] < (first + length)[:, None]
    ).astype(jnp.bfloat16)


def on_device(
    x_in,
    gate_input,
    in_b,
    in_c,
    step_size,
    log_decay,
    skip_gain,
    norm_gain,
    out_weight,
    probe,
    span_start,
    span_len,
    span_owner,
    span_label,
):
    tok = x_in.shape[0]
    local_attention_heads = step_size.shape[1]
    groups_here = in_b.shape[1] // STATE
    per_group = local_attention_heads // groups_here
    xs = x_in.astype(jnp.float32).reshape(tok, groups_here, per_group, HEAD_DIM)
    bmat = in_b.astype(jnp.float32).reshape(tok, groups_here, STATE)
    cmat = in_c.astype(jnp.float32).reshape(tok, groups_here, STATE)
    dtk = step_size.reshape(tok, groups_here, per_group)
    logd = log_decay.reshape(tok, groups_here, per_group)
    cum = jnp.cumsum(logd, axis=0)
    intra, local_state, total = piecewise_terms(xs, bmat, cmat, dtk, logd)
    state_in = exclusive_scan((local_state, total), "seq")
    ssm = (
        intra
        + inter_term(cmat, cum, state_in)
        + skip_gain.reshape(groups_here, per_group)[None, :, :, None] * xs
    )
    ssm = ssm.reshape(tok, groups_here, per_group * HEAD_DIM)
    gated = ssm * jax.nn.silu(
        gate_input.astype(jnp.float32).reshape(tok, groups_here, per_group * HEAD_DIM)
    )
    meansq = jnp.mean(gated * gated, axis=-1, keepdims=True)
    normalized_input = gated * lax.rsqrt(meansq + 1e-05)
    y_out = (normalized_input.reshape(tok, -1) * norm_gain[None, :]).astype(jnp.bfloat16)
    reach = min(tok, 128)
    next_rows = from_behind(y_out[:reach], "seq", -1)
    extended = jnp.concatenate([y_out, next_rows], axis=0)
    partial_out = jnp.dot(
        extended,
        lax.all_gather(out_weight, "seq", axis=1, tiled=True),
        preferred_element_type=jnp.float32,
    )
    projected = head_sum(partial_out.astype(jnp.bfloat16), "head")
    layer_out = projected[:tok]
    base = lax.axis_index("seq") * tok
    place = base + jnp.arange(tok + reach, dtype=jnp.int32)
    sums = jnp.dot(
        inside_mask(span_start, span_len, place), projected, preferred_element_type=jnp.float32
    )
    own_feature = (sums / span_len[:, None].astype(jnp.float32)).astype(jnp.bfloat16)
    count = span_start.shape[0]
    owners = lax.axis_size("seq")
    slots_total = owners * CAP
    owner = span_owner[:, 0]
    index = jnp.arange(count)
    earlier = index[None, :] < index[:, None]
    same = owner[:, None] == owner[None, :]
    slot = jnp.sum(jnp.logical_and(same, earlier), axis=1)
    target_labels = owner * CAP + slot
    pick = jnp.arange(slots_total, dtype=jnp.int32)[:, None] == target_labels[None, :]
    label_col = jnp.zeros((count, 128), jnp.bfloat16).at[:, 0].set(
        span_label.astype(jnp.bfloat16)
    )
    packed = jnp.concatenate([own_feature, label_col], axis=1)
    width = own_feature.shape[1]
    empty = jnp.zeros((1, packed.shape[1]), jnp.bfloat16).at[0, width].set(-1.0)
    chosen = jnp.where(jnp.any(pick, axis=1), jnp.argmax(pick, axis=1), count)
    send = jnp.concatenate([packed, empty], axis=0)[chosen].reshape(owners, CAP, -1)
    got = lax.all_to_all(send, "seq", split_axis=0, concat_axis=0, tiled=True)
    got = got.reshape(slots_total, -1)
    feature = got[:, :width]
    labels = got[:, width].astype(jnp.int32)
    valid = labels >= 0
    partial_logits = jnp.dot(feature, probe[0], preferred_element_type=jnp.float32)
    logits = partial_logits + lax.ppermute(partial_logits, "head", [(0, 1), (1, 0)])
    top = jnp.max(logits, axis=1, keepdims=True)
    lse = top[:, 0] + jnp.log(jnp.sum(jnp.exp(logits - top), axis=1))
    onehot = jnp.arange(logits.shape[1])[None, :] == labels[:, None]
    picked = jnp.sum(jnp.where(onehot, logits, 0.0), axis=1)
    loss = jnp.where(valid, lse - picked, 0.0)
    probs = jnp.exp(logits - lse[:, None])
    resid = jnp.where(valid[:, None], probs - onehot.astype(jnp.float32), 0.0).astype(jnp.bfloat16)
    grad = jnp.dot(feature.T, resid, preferred_element_type=jnp.float32)
    return (layer_out, grad[None], loss[None])


def solution(mesh):
    placed = (
        P("seq", "head"),
        P("seq", "head"),
        P("seq", "head"),
        P("seq", "head"),
        P("seq", "head"),
        P("seq", "head"),
        P("head"),
        P("head"),
        P("head", "seq"),
        P("seq", "head", None),
        P("seq"),
        P("seq"),
        P("seq", None),
        P("seq"),
    )
    return jax.shard_map(
        on_device,
        mesh=mesh,
        in_specs=placed,
        out_specs=(P("seq", "head"), P("seq", "head", None), P("seq", None)),
        check_vma=False,
    )
```

```python
import jax
import jax.numpy as jnp
from jax import lax
from jax.sharding import Mesh, PartitionSpec as P

HEAD_DIM = 64
STATE = 128
CAP = 2
SEQ = ("plane", "z")


def from_behind(value, axis, steps):
    count = lax.axis_size(axis)
    leading, last = (max(0, -steps), min(count, count - steps))
    return lax.ppermute(value, axis, [(source, source + steps) for source in range(leading, last)])


def segment_summands(xs, bmat, cmat, dtk, cum):
    high = lax.Precision.HIGHEST
    tok = xs.shape[0]
    cb = jnp.einsum("tgn,sgn->gts", cmat, bmat, precision=high)
    ordered = jnp.transpose(cum, (1, 2, 0))
    diff = ordered[:, :, :, None] - ordered[:, :, None, :]
    lower = jnp.arange(tok)[:, None] >= jnp.arange(tok)[None, :]
    decay = jnp.where(lower, jnp.exp(jnp.where(lower, diff, 0.0)), 0.0)
    weights = cb[:, None] * decay * jnp.transpose(dtk, (1, 2, 0))[:, :, None, :]
    intra = jnp.einsum("gkts,sgkp->tgkp", weights, xs, precision=high)
    tail = jnp.exp(cum[-1][None] - cum) * dtk
    local_state = jnp.einsum("tgk,tgkp,tgn->gkpn", tail, xs, bmat, precision=high)
    return (intra, local_state, cum[-1])


def inter_term(cmat, cum, state_in):
    high = lax.Precision.HIGHEST
    return jnp.exp(cum)[..., None] * jnp.einsum("tgn,gkpn->tgkp", cmat, state_in, precision=high)


def piecewise_terms(xs, bmat, cmat, dtk, logd):
    tok = xs.shape[0]
    width = min(tok, 256)
    pieces = tok // width
    state = jnp.zeros((xs.shape[1], xs.shape[2], xs.shape[3], bmat.shape[2]), jnp.float32)
    total = jnp.zeros((xs.shape[1], xs.shape[2]), jnp.float32)
    results = []
    for piece in range(pieces):
        lower_edge = piece * width
        upper_edge = lower_edge + width
        inner_cum = jnp.cumsum(logd[lower_edge:upper_edge], axis=0)
        intra, local_state, piece_total = segment_summands(
            xs[lower_edge:upper_edge],
            bmat[lower_edge:upper_edge],
            cmat[lower_edge:upper_edge],
            dtk[lower_edge:upper_edge],
            inner_cum,
        )
        results.append(intra + inter_term(cmat[lower_edge:upper_edge], inner_cum, state))
        state = state * jnp.exp(piece_total)[..., None, None] + local_state
        total = total + piece_total
    return (jnp.concatenate(results, axis=0), state, total)


def exclusive_scan(part, axis):
    count = lax.axis_size(axis)
    place = lax.axis_index(axis)
    inclusive = part
    exclusive = None
    step = 1
    while step < count:
        pairs = [(source, source + step) for source in range(count - step)]
        got = jax.tree.map(lambda a: lax.ppermute(a, axis, pairs), inclusive)
        exclusive = got if exclusive is None else combine_states(got, exclusive)
        if step * 2 < count:
            inclusive = combine_states(got, inclusive)
        step *= 2
    return exclusive[0]

def combine_states(earlier, later):
    return (earlier[0] * jnp.exp(later[1])[..., None, None] + later[0], earlier[1] + later[1])


def head_sum(part, axis):
    half = part.shape[1] // 2
    me = lax.axis_index(axis)
    mine = lax.dynamic_slice_in_dim(part, me * half, half, axis=1)
    other = lax.dynamic_slice_in_dim(part, (1 - me) * half, half, axis=1)
    got = lax.ppermute(other, axis, [(0, 1), (1, 0)])
    return (mine.astype(jnp.float32) + got.astype(jnp.float32)).astype(jnp.bfloat16)


def grouped_projection(y_out, out_weight, reach):
    tok = y_out.shape[0]
    groups = lax.axis_size("z")
    planes = lax.axis_size("plane")
    gathered_weight = lax.all_gather(out_weight, "plane", axis=1, tiled=True)
    group_rows = lax.all_gather(y_out, "z", axis=0, tiled=True)
    first = y_out[:reach]
    extra = None
    for target in range(groups):
        pairs = [((p + 1) * groups, p * groups + target) for p in range(planes - 1)]
        got = lax.ppermute(first, SEQ, pairs)
        extra = got if extra is None else extra + got
    extended = jnp.concatenate([group_rows, extra], axis=0)
    part = jnp.dot(extended, gathered_weight, preferred_element_type=jnp.float32)
    summed = head_sum(part.astype(jnp.bfloat16), "head")
    send = jnp.stack([summed[z * tok : z * tok + tok + reach] for z in range(groups)])
    back = lax.all_to_all(send, "z", 0, 0, tiled=True)
    blocks = summed.shape[1] // 128
    back = back.reshape(groups, tok + reach, blocks, 128)
    return jnp.transpose(back, (1, 2, 0, 3)).reshape(tok + reach, groups * blocks * 128)

def inside_mask(first, length, place):
    return jnp.logical_and(
        place[None, :] >= first[:, None], place[None, :] < (first + length)[:, None]
    ).astype(jnp.bfloat16)


def on_device(
    x_in,
    gate_input,
    in_b,
    in_c,
    step_size,
    log_decay,
    skip_gain,
    norm_gain,
    out_weight,
    probe,
    span_start,
    span_len,
    span_owner,
    span_label,
):
    tok = x_in.shape[0]
    local_attention_heads = step_size.shape[1]
    groups_here = in_b.shape[1] // STATE
    per_group = local_attention_heads // groups_here
    xs = x_in.astype(jnp.float32).reshape(tok, groups_here, per_group, HEAD_DIM)
    bmat = in_b.astype(jnp.float32).reshape(tok, groups_here, STATE)
    cmat = in_c.astype(jnp.float32).reshape(tok, groups_here, STATE)
    dtk = step_size.reshape(tok, groups_here, per_group)
    logd = log_decay.reshape(tok, groups_here, per_group)
    cum = jnp.cumsum(logd, axis=0)
    intra, local_state, total = piecewise_terms(xs, bmat, cmat, dtk, logd)
    state_in = exclusive_scan((local_state, total), SEQ)
    ssm = (
        intra
        + inter_term(cmat, cum, state_in)
        + skip_gain.reshape(groups_here, per_group)[None, :, :, None] * xs
    )
    ssm = ssm.reshape(tok, groups_here, per_group * HEAD_DIM)
    gated = ssm * jax.nn.silu(
        gate_input.astype(jnp.float32).reshape(tok, groups_here, per_group * HEAD_DIM)
    )
    meansq = jnp.mean(gated * gated, axis=-1, keepdims=True)
    normalized_input = gated * lax.rsqrt(meansq + 1e-05)
    y_out = (normalized_input.reshape(tok, -1) * norm_gain[None, :]).astype(jnp.bfloat16)
    reach = min(tok, 128)
    projected = grouped_projection(y_out, out_weight, reach)
    layer_out = projected[:tok]
    base = lax.axis_index(SEQ) * tok
    place = base + jnp.arange(tok + reach, dtype=jnp.int32)
    sums = jnp.dot(
        inside_mask(span_start, span_len, place), projected, preferred_element_type=jnp.float32
    )
    own_feature = (sums / span_len[:, None].astype(jnp.float32)).astype(jnp.bfloat16)
    count = span_start.shape[0]
    owners = lax.axis_size(SEQ)
    slots_total = owners * CAP
    owner = span_owner[:, 0]
    index = jnp.arange(count)
    earlier = index[None, :] < index[:, None]
    same = owner[:, None] == owner[None, :]
    slot = jnp.sum(jnp.logical_and(same, earlier), axis=1)
    target_labels = owner * CAP + slot
    pick = jnp.arange(slots_total, dtype=jnp.int32)[:, None] == target_labels[None, :]
    label_col = jnp.zeros((count, 128), jnp.bfloat16).at[:, 0].set(
        span_label.astype(jnp.bfloat16)
    )
    packed = jnp.concatenate([own_feature, label_col], axis=1)
    width = own_feature.shape[1]
    empty = jnp.zeros((1, packed.shape[1]), jnp.bfloat16).at[0, width].set(-1.0)
    chosen = jnp.where(jnp.any(pick, axis=1), jnp.argmax(pick, axis=1), count)
    send = jnp.concatenate([packed, empty], axis=0)[chosen].reshape(owners, CAP, -1)
    got = lax.all_to_all(send, SEQ, split_axis=0, concat_axis=0, tiled=True)
    got = got.reshape(slots_total, -1)
    feature = got[:, :width]
    labels = got[:, width].astype(jnp.int32)
    valid = labels >= 0
    partial_logits = jnp.dot(feature, probe[0], preferred_element_type=jnp.float32)
    logits = partial_logits + lax.ppermute(partial_logits, "head", [(0, 1), (1, 0)])
    top = jnp.max(logits, axis=1, keepdims=True)
    lse = top[:, 0] + jnp.log(jnp.sum(jnp.exp(logits - top), axis=1))
    onehot = jnp.arange(logits.shape[1])[None, :] == labels[:, None]
    picked = jnp.sum(jnp.where(onehot, logits, 0.0), axis=1)
    loss = jnp.where(valid, lse - picked, 0.0)
    probs = jnp.exp(logits - lse[:, None])
    resid = jnp.where(valid[:, None], probs - onehot.astype(jnp.float32), 0.0).astype(jnp.bfloat16)
    grad = jnp.dot(feature.T, resid, preferred_element_type=jnp.float32)
    return (layer_out, grad[None], loss[None])


def solution(mesh):
    placed = (
        P(SEQ, "head"),
        P(SEQ, "head"),
        P(SEQ, "head"),
        P(SEQ, "head"),
        P(SEQ, "head"),
        P(SEQ, "head"),
        P("head"),
        P("head"),
        P("head", SEQ),
        P(SEQ, "head", None),
        P(SEQ),
        P(SEQ),
        P(SEQ, None),
        P(SEQ),
    )
    seq_count, head_count = mesh.devices.shape
    group = 4 if seq_count % 4 == 0 else 1
    grid = Mesh(mesh.devices.reshape(seq_count // group, group, head_count), ("plane", "z", "head"))
    return jax.shard_map(
        on_device,
        mesh=grid,
        in_specs=placed,
        out_specs=(P(SEQ, "head"), P(SEQ, "head", None), P(SEQ, None)),
        check_vma=False,
    )
```

```python
import jax
import jax.numpy as jnp
from jax import lax
from jax.sharding import Mesh, PartitionSpec as P

HEAD_DIM = 64
STATE = 128
CAP = 2
SEQ = ("plane", "z")


def from_behind(value, axis, steps):
    count = lax.axis_size(axis)
    leading, last = (max(0, -steps), min(count, count - steps))
    return lax.ppermute(value, axis, [(source, source + steps) for source in range(leading, last)])


def segment_summands(xs, bmat, cmat, dtk, cum):
    high = lax.Precision.HIGHEST
    tok = xs.shape[0]
    cb = jnp.einsum("tgn,sgn->gts", cmat, bmat, precision=high)
    ordered = jnp.transpose(cum, (1, 2, 0))
    diff = ordered[:, :, :, None] - ordered[:, :, None, :]
    lower = jnp.arange(tok)[:, None] >= jnp.arange(tok)[None, :]
    decay = jnp.where(lower, jnp.exp(jnp.where(lower, diff, 0.0)), 0.0)
    weights = cb[:, None] * decay * jnp.transpose(dtk, (1, 2, 0))[:, :, None, :]
    intra = jnp.einsum("gkts,sgkp->tgkp", weights, xs, precision=high)
    tail = jnp.exp(cum[-1][None] - cum) * dtk
    local_state = jnp.einsum("tgk,tgkp,tgn->gkpn", tail, xs, bmat, precision=high)
    return (intra, local_state, cum[-1])


def inter_term(cmat, cum, state_in):
    high = lax.Precision.HIGHEST
    return jnp.exp(cum)[..., None] * jnp.einsum("tgn,gkpn->tgkp", cmat, state_in, precision=high)


def piecewise_terms(xs, bmat, cmat, dtk, logd):
    tok = xs.shape[0]
    width = min(tok, 256)
    pieces = tok // width
    state = jnp.zeros((xs.shape[1], xs.shape[2], xs.shape[3], bmat.shape[2]), jnp.float32)
    total = jnp.zeros((xs.shape[1], xs.shape[2]), jnp.float32)
    results = []
    for piece in range(pieces):
        lower_edge = piece * width
        upper_edge = lower_edge + width
        inner_cum = jnp.cumsum(logd[lower_edge:upper_edge], axis=0)
        intra, local_state, piece_total = segment_summands(
            xs[lower_edge:upper_edge],
            bmat[lower_edge:upper_edge],
            cmat[lower_edge:upper_edge],
            dtk[lower_edge:upper_edge],
            inner_cum,
        )
        results.append(intra + inter_term(cmat[lower_edge:upper_edge], inner_cum, state))
        state = state * jnp.exp(piece_total)[..., None, None] + local_state
        total = total + piece_total
    return (jnp.concatenate(results, axis=0), state, total)


def exclusive_scan(part, axis):
    count = lax.axis_size(axis)
    place = lax.axis_index(axis)
    inclusive = part
    exclusive = None
    step = 1
    while step < count:
        pairs = [(source, source + step) for source in range(count - step)]
        got = jax.tree.map(lambda a: lax.ppermute(a, axis, pairs), inclusive)
        exclusive = got if exclusive is None else combine_states(got, exclusive)
        if step * 2 < count:
            inclusive = combine_states(got, inclusive)
        step *= 2
    return exclusive[0]

def combine_states(earlier, later):
    return (earlier[0] * jnp.exp(later[1])[..., None, None] + later[0], earlier[1] + later[1])


def head_sum(part, axis):
    half = part.shape[1] // 2
    me = lax.axis_index(axis)
    mine = lax.dynamic_slice_in_dim(part, me * half, half, axis=1)
    other = lax.dynamic_slice_in_dim(part, (1 - me) * half, half, axis=1)
    got = lax.ppermute(other, axis, [(0, 1), (1, 0)])
    return (mine.astype(jnp.float32) + got.astype(jnp.float32)).astype(jnp.bfloat16)


def grouped_projection(y_out, out_weight, reach):
    tok = y_out.shape[0]
    groups = lax.axis_size("z")
    planes = lax.axis_size("plane")
    gathered_weight = lax.all_gather(out_weight, "plane", axis=1, tiled=True)
    me = lax.axis_index("z")

    def around(value, shift):
        pairs = [(p * groups + z, p * groups + (z + shift) % groups) for p in range(planes) for z in range(groups)]
        return lax.ppermute(value, SEQ, pairs)

    received = jnp.stack([y_out] + [around(y_out, s) for s in range(1, groups)])
    order = (me - jnp.arange(groups)) % groups
    group_rows = jnp.take(received, order, axis=0).reshape(groups * tok, -1)
    first = y_out[:reach]
    extra = None
    for target in range(groups):
        pairs = [((p + 1) * groups, p * groups + target) for p in range(planes - 1)]
        got = lax.ppermute(first, SEQ, pairs)
        extra = got if extra is None else extra + got
    extended = jnp.concatenate([group_rows, extra], axis=0)
    part = jnp.dot(extended, gathered_weight, preferred_element_type=jnp.float32)
    summed = head_sum(part.astype(jnp.bfloat16), "head")
    chunks = [
        around(lax.dynamic_slice_in_dim(summed, ((me + s) % groups) * tok, tok + reach, 0), s)
        for s in range(1, groups)
    ]
    own = lax.dynamic_slice_in_dim(summed, me * tok, tok + reach, 0)
    back = jnp.take(jnp.stack([own] + chunks), order, axis=0)
    blocks = summed.shape[1] // 128
    back = back.reshape(groups, tok + reach, blocks, 128)
    return jnp.transpose(back, (1, 2, 0, 3)).reshape(tok + reach, groups * blocks * 128)

def inside_mask(first, length, place):
    return jnp.logical_and(
        place[None, :] >= first[:, None], place[None, :] < (first + length)[:, None]
    ).astype(jnp.bfloat16)


def on_device(
    x_in,
    gate_input,
    in_b,
    in_c,
    step_size,
    log_decay,
    skip_gain,
    norm_gain,
    out_weight,
    probe,
    span_start,
    span_len,
    span_owner,
    span_label,
):
    tok = x_in.shape[0]
    local_attention_heads = step_size.shape[1]
    groups_here = in_b.shape[1] // STATE
    per_group = local_attention_heads // groups_here
    xs = x_in.astype(jnp.float32).reshape(tok, groups_here, per_group, HEAD_DIM)
    bmat = in_b.astype(jnp.float32).reshape(tok, groups_here, STATE)
    cmat = in_c.astype(jnp.float32).reshape(tok, groups_here, STATE)
    dtk = step_size.reshape(tok, groups_here, per_group)
    logd = log_decay.reshape(tok, groups_here, per_group)
    cum = jnp.cumsum(logd, axis=0)
    intra, local_state, total = piecewise_terms(xs, bmat, cmat, dtk, logd)
    state_in = exclusive_scan((local_state, total), SEQ)
    ssm = (
        intra
        + inter_term(cmat, cum, state_in)
        + skip_gain.reshape(groups_here, per_group)[None, :, :, None] * xs
    )
    ssm = ssm.reshape(tok, groups_here, per_group * HEAD_DIM)
    gated = ssm * jax.nn.silu(
        gate_input.astype(jnp.float32).reshape(tok, groups_here, per_group * HEAD_DIM)
    )
    meansq = jnp.mean(gated * gated, axis=-1, keepdims=True)
    normalized_input = gated * lax.rsqrt(meansq + 1e-05)
    y_out = (normalized_input.reshape(tok, -1) * norm_gain[None, :]).astype(jnp.bfloat16)
    reach = min(tok, 128)
    projected = grouped_projection(y_out, out_weight, reach)
    layer_out = projected[:tok]
    base = lax.axis_index(SEQ) * tok
    place = base + jnp.arange(tok + reach, dtype=jnp.int32)
    sums = jnp.dot(
        inside_mask(span_start, span_len, place), projected, preferred_element_type=jnp.float32
    )
    own_feature = (sums / span_len[:, None].astype(jnp.float32)).astype(jnp.bfloat16)
    count = span_start.shape[0]
    owners = lax.axis_size(SEQ)
    slots_total = owners * CAP
    owner = span_owner[:, 0]
    index = jnp.arange(count)
    earlier = index[None, :] < index[:, None]
    same = owner[:, None] == owner[None, :]
    slot = jnp.sum(jnp.logical_and(same, earlier), axis=1)
    target_labels = owner * CAP + slot
    pick = jnp.arange(slots_total, dtype=jnp.int32)[:, None] == target_labels[None, :]
    label_col = jnp.zeros((count, 128), jnp.bfloat16).at[:, 0].set(
        span_label.astype(jnp.bfloat16)
    )
    packed = jnp.concatenate([own_feature, label_col], axis=1)
    width = own_feature.shape[1]
    empty = jnp.zeros((1, packed.shape[1]), jnp.bfloat16).at[0, width].set(-1.0)
    chosen = jnp.where(jnp.any(pick, axis=1), jnp.argmax(pick, axis=1), count)
    send = jnp.concatenate([packed, empty], axis=0)[chosen].reshape(owners, CAP, -1)
    got = lax.all_to_all(send, SEQ, split_axis=0, concat_axis=0, tiled=True)
    got = got.reshape(slots_total, -1)
    feature = got[:, :width]
    labels = got[:, width].astype(jnp.int32)
    valid = labels >= 0
    partial_logits = jnp.dot(feature, probe[0], preferred_element_type=jnp.float32)
    logits = partial_logits + lax.ppermute(partial_logits, "head", [(0, 1), (1, 0)])
    top = jnp.max(logits, axis=1, keepdims=True)
    lse = top[:, 0] + jnp.log(jnp.sum(jnp.exp(logits - top), axis=1))
    onehot = jnp.arange(logits.shape[1])[None, :] == labels[:, None]
    picked = jnp.sum(jnp.where(onehot, logits, 0.0), axis=1)
    loss = jnp.where(valid, lse - picked, 0.0)
    probs = jnp.exp(logits - lse[:, None])
    resid = jnp.where(valid[:, None], probs - onehot.astype(jnp.float32), 0.0).astype(jnp.bfloat16)
    grad = jnp.dot(feature.T, resid, preferred_element_type=jnp.float32)
    return (layer_out, grad[None], loss[None])


def solution(mesh):
    placed = (
        P(SEQ, "head"),
        P(SEQ, "head"),
        P(SEQ, "head"),
        P(SEQ, "head"),
        P(SEQ, "head"),
        P(SEQ, "head"),
        P("head"),
        P("head"),
        P("head", SEQ),
        P(SEQ, "head", None),
        P(SEQ),
        P(SEQ),
        P(SEQ, None),
        P(SEQ),
    )
    seq_count, head_count = mesh.devices.shape
    group = 4 if seq_count % 4 == 0 else 1
    grid = Mesh(mesh.devices.reshape(seq_count // group, group, head_count), ("plane", "z", "head"))
    return jax.shard_map(
        on_device,
        mesh=grid,
        in_specs=placed,
        out_specs=(P(SEQ, "head"), P(SEQ, "head", None), P(SEQ, None)),
        check_vma=False,
    )
```

```python
import jax
import jax.numpy as jnp
from jax import lax
from jax.sharding import PartitionSpec as P

HEAD_DIM = 64
STATE = 128
CAP = 2


def from_behind(value, axis, steps):
    count = lax.axis_size(axis)
    leading, last = (max(0, -steps), min(count, count - steps))
    return lax.ppermute(value, axis, [(source, source + steps) for source in range(leading, last)])


def segment_summands(xs, bmat, cmat, dtk, cum):
    high = lax.Precision.HIGHEST
    tok = xs.shape[0]
    cb = jnp.einsum("tgn,sgn->gts", cmat, bmat, precision=high)
    ordered = jnp.transpose(cum, (1, 2, 0))
    diff = ordered[:, :, :, None] - ordered[:, :, None, :]
    lower = jnp.arange(tok)[:, None] >= jnp.arange(tok)[None, :]
    decay = jnp.where(lower, jnp.exp(jnp.where(lower, diff, 0.0)), 0.0)
    weights = cb[:, None] * decay * jnp.transpose(dtk, (1, 2, 0))[:, :, None, :]
    intra = jnp.einsum("gkts,sgkp->tgkp", weights, xs, precision=high)
    tail = jnp.exp(cum[-1][None] - cum) * dtk
    local_state = jnp.einsum("tgk,tgkp,tgn->gkpn", tail, xs, bmat, precision=high)
    return (intra, local_state, cum[-1])


def inter_term(cmat, cum, state_in):
    high = lax.Precision.HIGHEST
    return jnp.exp(cum)[..., None] * jnp.einsum("tgn,gkpn->tgkp", cmat, state_in, precision=high)


def piecewise_terms(xs, bmat, cmat, dtk, logd):
    tok = xs.shape[0]
    width = min(tok, 256)
    pieces = tok // width
    state = jnp.zeros((xs.shape[1], xs.shape[2], xs.shape[3], bmat.shape[2]), jnp.float32)
    total = jnp.zeros((xs.shape[1], xs.shape[2]), jnp.float32)
    results = []
    for piece in range(pieces):
        lower_edge = piece * width
        upper_edge = lower_edge + width
        inner_cum = jnp.cumsum(logd[lower_edge:upper_edge], axis=0)
        intra, local_state, piece_total = segment_summands(
            xs[lower_edge:upper_edge],
            bmat[lower_edge:upper_edge],
            cmat[lower_edge:upper_edge],
            dtk[lower_edge:upper_edge],
            inner_cum,
        )
        results.append(intra + inter_term(cmat[lower_edge:upper_edge], inner_cum, state))
        state = state * jnp.exp(piece_total)[..., None, None] + local_state
        total = total + piece_total
    return (jnp.concatenate(results, axis=0), state, total)


def exclusive_scan(part, axis):
    count = lax.axis_size(axis)
    place = lax.axis_index(axis)
    inclusive = part
    exclusive = None
    step = 1
    while step < count:
        pairs = [(source, source + step) for source in range(count - step)]
        got = jax.tree.map(lambda a: lax.ppermute(a, axis, pairs), inclusive)
        exclusive = got if exclusive is None else combine_states(got, exclusive)
        if step * 2 < count:
            inclusive = combine_states(got, inclusive)
        step *= 2
    return exclusive[0]

def combine_states(earlier, later):
    return (earlier[0] * jnp.exp(later[1])[..., None, None] + later[0], earlier[1] + later[1])


def head_sum(part, axis):
    half = part.shape[1] // 2
    me = lax.axis_index(axis)
    mine = lax.dynamic_slice_in_dim(part, me * half, half, axis=1)
    other = lax.dynamic_slice_in_dim(part, (1 - me) * half, half, axis=1)
    got = lax.ppermute(other, axis, [(0, 1), (1, 0)])
    return (mine.astype(jnp.float32) + got.astype(jnp.float32)).astype(jnp.bfloat16)

def inside_mask(first, length, place):
    return jnp.logical_and(
        place[None, :] >= first[:, None], place[None, :] < (first + length)[:, None]
    ).astype(jnp.bfloat16)


def on_device(
    x_in,
    gate_input,
    in_b,
    in_c,
    step_size,
    log_decay,
    skip_gain,
    norm_gain,
    out_weight,
    probe,
    span_start,
    span_len,
    span_owner,
    span_label,
):
    tok = x_in.shape[0]
    local_attention_heads = step_size.shape[1]
    groups_here = in_b.shape[1] // STATE
    per_group = local_attention_heads // groups_here
    xs = x_in.astype(jnp.float32).reshape(tok, groups_here, per_group, HEAD_DIM)
    bmat = in_b.astype(jnp.float32).reshape(tok, groups_here, STATE)
    cmat = in_c.astype(jnp.float32).reshape(tok, groups_here, STATE)
    dtk = step_size.reshape(tok, groups_here, per_group)
    logd = log_decay.reshape(tok, groups_here, per_group)
    cum = jnp.cumsum(logd, axis=0)
    intra, local_state, total = piecewise_terms(xs, bmat, cmat, dtk, logd)
    state_in = exclusive_scan((local_state, total), "seq")
    ssm = (
        intra
        + inter_term(cmat, cum, state_in)
        + skip_gain.reshape(groups_here, per_group)[None, :, :, None] * xs
    )
    ssm = ssm.reshape(tok, groups_here, per_group * HEAD_DIM)
    gated = ssm * jax.nn.silu(
        gate_input.astype(jnp.float32).reshape(tok, groups_here, per_group * HEAD_DIM)
    )
    meansq = jnp.mean(gated * gated, axis=-1, keepdims=True)
    normalized_input = gated * lax.rsqrt(meansq + 1e-05)
    y_out = (normalized_input.reshape(tok, -1) * norm_gain[None, :]).astype(jnp.bfloat16)
    reach = min(tok, 128)
    next_rows = from_behind(y_out[:reach], "seq", -1)
    extended = jnp.concatenate([y_out, next_rows], axis=0)
    weight = lax.all_gather(out_weight, "seq", axis=1, tiled=True)
    half = weight.shape[1] // 2
    me = lax.axis_index("head")

    def columns(index):
        block = lax.dynamic_slice_in_dim(weight, index * half, half, axis=1)
        return jnp.dot(extended, block, preferred_element_type=jnp.float32).astype(jnp.bfloat16)

    got = lax.ppermute(columns(1 - me), "head", [(0, 1), (1, 0)])
    projected = (columns(me).astype(jnp.float32) + got.astype(jnp.float32)).astype(jnp.bfloat16)
    layer_out = projected[:tok]
    base = lax.axis_index("seq") * tok
    place = base + jnp.arange(tok + reach, dtype=jnp.int32)
    sums = jnp.dot(
        inside_mask(span_start, span_len, place), projected, preferred_element_type=jnp.float32
    )
    own_feature = (sums / span_len[:, None].astype(jnp.float32)).astype(jnp.bfloat16)
    count = span_start.shape[0]
    owners = lax.axis_size("seq")
    slots_total = owners * CAP
    owner = span_owner[:, 0]
    index = jnp.arange(count)
    earlier = index[None, :] < index[:, None]
    same = owner[:, None] == owner[None, :]
    slot = jnp.sum(jnp.logical_and(same, earlier), axis=1)
    target_labels = owner * CAP + slot
    pick = jnp.arange(slots_total, dtype=jnp.int32)[:, None] == target_labels[None, :]
    label_col = jnp.zeros((count, 128), jnp.bfloat16).at[:, 0].set(
        span_label.astype(jnp.bfloat16)
    )
    packed = jnp.concatenate([own_feature, label_col], axis=1)
    width = own_feature.shape[1]
    empty = jnp.zeros((1, packed.shape[1]), jnp.bfloat16).at[0, width].set(-1.0)
    chosen = jnp.where(jnp.any(pick, axis=1), jnp.argmax(pick, axis=1), count)
    send = jnp.concatenate([packed, empty], axis=0)[chosen].reshape(owners, CAP, -1)
    got = lax.all_to_all(send, "seq", split_axis=0, concat_axis=0, tiled=True)
    got = got.reshape(slots_total, -1)
    feature = got[:, :width]
    labels = got[:, width].astype(jnp.int32)
    valid = labels >= 0
    partial_logits = jnp.dot(feature, probe[0], preferred_element_type=jnp.float32)
    logits = partial_logits + lax.ppermute(partial_logits, "head", [(0, 1), (1, 0)])
    top = jnp.max(logits, axis=1, keepdims=True)
    lse = top[:, 0] + jnp.log(jnp.sum(jnp.exp(logits - top), axis=1))
    onehot = jnp.arange(logits.shape[1])[None, :] == labels[:, None]
    picked = jnp.sum(jnp.where(onehot, logits, 0.0), axis=1)
    loss = jnp.where(valid, lse - picked, 0.0)
    probs = jnp.exp(logits - lse[:, None])
    resid = jnp.where(valid[:, None], probs - onehot.astype(jnp.float32), 0.0).astype(jnp.bfloat16)
    grad = jnp.dot(feature.T, resid, preferred_element_type=jnp.float32)
    return (layer_out, grad[None], loss[None])


def solution(mesh):
    placed = (
        P("seq", "head"),
        P("seq", "head"),
        P("seq", "head"),
        P("seq", "head"),
        P("seq", "head"),
        P("seq", "head"),
        P("head"),
        P("head"),
        P("head", "seq"),
        P("seq", "head", None),
        P("seq"),
        P("seq"),
        P("seq", None),
        P("seq"),
    )
    return jax.shard_map(
        on_device,
        mesh=mesh,
        in_specs=placed,
        out_specs=(P("seq", "head"), P("seq", "head", None), P("seq", None)),
        check_vma=False,
    )
```
